256 devices in a mesh: dict: 16 (over x, z_hi, core), tensor: 16 (over z_lo, y).
Axes of the slice: x: 4, y: 4, z: 8 (z_hi: 2, z_lo: 4; z = z_hi * 4 + z_lo), core: 2. Of those that a mesh axis runs over, the one named last changes fastest.
Arguments:
- residual: bfloat16 [4096, 8192], P('dict', 'tensor'), may hold values from -10 to 10
- norm_gain: float32 [8192], replicated, may hold values from 0.1 to 1.9
- w_query: bfloat16 [8192, 8192], P('dict', 'tensor'), may hold values from -2 to 2
- w_key: bfloat16 [8192, 1024], P('dict'), may hold values from -2 to 2
- value_weight: bfloat16 [8192, 1024], P('dict'), may hold values from -0.0625 to 0.0625
- w_out: bfloat16 [8192, 8192], P('tensor', 'dict'), may hold values from -0.0625 to 0.0625
- decoder: bfloat16 [131072, 8192], P('dict', 'tensor'), may hold values from -0.5 to 0.5
- block_ids: int32 [2], replicated, may hold values from 0 to 1023, as said below
- latent_ids: int32 [4096, 64], P('dict'), may hold values from 0 to 131071, as said below
- latent_vals: float32 [4096, 64], P('dict'), may hold values from 0.5 to 4
- prompt_lens: int32 [16], P('dict'), may hold values from 32 to 256, as said below
Outputs:
- ablations: bfloat16 [2, 4096, 8192], P(None, 'dict', 'tensor')
The draws below stay inside these ranges and needn't reach their ends.
Inputs may be any that keep to these rules, and one draw needn't show every extreme that they name: `block_ids`: 2 distinct blocks, one of them the last block; block b covers latents b * 128 to b * 128 + 127. `latent_ids`: about half of a row's entries name latents of the swept blocks; a row may name a latent more than once. Prompt p uses its first prompt_lens[p] rows; some prompt uses all 256 and some only 32.
All inputs are finite; a program needn't handle non-finite values.
Results may differ from the reference program's by a relative error of at most 0.009.
Values may be sent and summed in bfloat16 or wider, within the bound.
No kernel may reach another device: no remote copies, remote signals or barrier semaphores. Data moves between devices by JAX's collectives and lax.ppermute only.
A program may use at most 192 MiB of HBM per device.

```python
import math
import jax
import jax.numpy as jnp
from jax import lax

MODEL_WIDTH = 8192
QUERY_HEADS = 64
KEY_VALUE_HEADS = 8
HEAD_SIZE = 128
BLOCK = 128
TOPK = 64
PROMPT_ROWS = 256
ABLATION_STEPS = 2
ROWS = 4096
PROMPTS = 16
LATENTS = 131072
N_TENSOR = 16


def sweep_blocks(base_key):
    block_total = LATENTS // BLOCK
    shuffled = jax.random.permutation(jax.random.fold_in(base_key, 11), block_total - 1)
    chosen_blocks = jnp.concatenate([shuffled[:ABLATION_STEPS - 1].astype(jnp.int32), jnp.full((1,), block_total - 1, jnp.int32)])
    order = jax.random.permutation(jax.random.fold_in(base_key, 13), ABLATION_STEPS)
    return chosen_blocks[order].astype(jnp.int32)


def draw_block_ids(key, part):
    return sweep_blocks(key)


def draw_latent_ids(key, part):
    blocks_used = sweep_blocks(key)
    key_spread, key_chosen, key_within, key_picked = jax.random.split(jax.random.fold_in(key, 23), 4)
    spread = jax.random.randint(key_spread, (ROWS, TOPK), 0, LATENTS)
    chosen = jax.random.randint(key_chosen, (ROWS, TOPK), 0, ABLATION_STEPS)
    within = jax.random.randint(key_within, (ROWS, TOPK), 0, BLOCK)
    picked = jax.random.randint(key_picked, (ROWS, TOPK), 0, 2)
    targeted = blocks_used[chosen] * BLOCK + within
    return jnp.where(picked == 1, targeted, spread).astype(jnp.int32)


def draw_prompt_lens(key, part):
    key_lengths, key_shuffle = jax.random.split(jax.random.fold_in(key, 37))
    lengths = jax.random.randint(key_lengths, (PROMPTS,), PROMPT_ROWS // 8, PROMPT_ROWS + 1)
    shuffled = jax.random.permutation(key_shuffle, PROMPTS)
    lengths = lengths.at[shuffled[0]].set(PROMPT_ROWS)
    lengths = lengths.at[shuffled[1]].set(PROMPT_ROWS // 8)
    return lengths.astype(jnp.int32)


def planted(key):
    base = jax.random.fold_in(key, 61)
    key_sign, key_direction, key_query, key_value_random = jax.random.split(base, 4)
    signs = (2 * jax.random.randint(key_sign, (MODEL_WIDTH,), 0, 2) - 1).astype(jnp.float32)
    attention_pattern = (2 * jax.random.randint(key_direction, (KEY_VALUE_HEADS, HEAD_SIZE), 0, 2) - 1).astype(jnp.float32)
    dims = jnp.arange(HEAD_SIZE, dtype=jnp.int32) % (HEAD_SIZE // 2)
    attention_pattern = jnp.where((dims >= HEAD_SIZE // 4)[None, :], attention_pattern, jnp.zeros_like(attention_pattern))
    key_amplitude = jax.random.uniform(key_value_random, (KEY_VALUE_HEADS,), jnp.float32, 3.0, 5.0)
    targets = jnp.exp(jax.random.uniform(key_query, (QUERY_HEADS,), jnp.float32, 5.0106, 6.3969))
    query_group_index = jnp.arange(QUERY_HEADS, dtype=jnp.int32) // (QUERY_HEADS // KEY_VALUE_HEADS)
    query_amp = 2.0 * targets / (key_amplitude[query_group_index] * HEAD_SIZE ** 0.5)
    return (signs, attention_pattern, key_amplitude, query_amp, query_group_index)


def base_feature_map(key, rows, cols):
    return jnp.clip(jax.random.normal(key, (rows, cols), jnp.float32), -4.0, 4.0)


def draw_residual(key, part):
    signs = planted(key)[0]
    key_noise, key_pick = jax.random.split(jax.random.fold_in(key, 71), 2)
    positions = jnp.arange(ROWS, dtype=jnp.int32) % PROMPT_ROWS
    heavy = (positions == 0) | (jax.random.randint(key_pick, (ROWS,), 0, 8) == 0)
    noise = jnp.clip(jax.random.normal(key_noise, (ROWS, MODEL_WIDTH), jnp.float32), -6.0, 6.0)
    lift = jnp.where(heavy, 3.0, 0.0)[:, None] * signs[None, :]
    return (noise + lift).astype(jnp.bfloat16)


def draw_w_query(key, part):
    signs, attention_pattern, key_amplitude, query_amp, query_group_index = planted(key)
    feature_map = base_feature_map(jax.random.fold_in(key, 83), MODEL_WIDTH, QUERY_HEADS * HEAD_SIZE)
    raised_rows = (query_amp[:, None] * attention_pattern[query_group_index]).reshape(QUERY_HEADS * HEAD_SIZE)
    return (feature_map / MODEL_WIDTH ** 0.5 + signs[:, None] * raised_rows[None, :] / MODEL_WIDTH).astype(jnp.bfloat16)


def draw_w_key(key, part):
    signs, attention_pattern, key_amplitude, query_amp, query_group_index = planted(key)
    feature_map = base_feature_map(jax.random.fold_in(key, 89), MODEL_WIDTH, KEY_VALUE_HEADS * HEAD_SIZE)
    raised_rows = (key_amplitude[:, None] * attention_pattern).reshape(KEY_VALUE_HEADS * HEAD_SIZE)
    return (feature_map / MODEL_WIDTH ** 0.5 + signs[:, None] * raised_rows[None, :] / MODEL_WIDTH).astype(jnp.bfloat16)


def steps_of(key, shape, cuts, low, top_value):
    level = 1.0
    for axis_at, shards_of in cuts:
        steps = jax.random.uniform(jax.random.fold_in(jax.random.fold_in(key, 6), axis_at), (shards_of,), jnp.float32, low / len(cuts), top_value / len(cuts))
        level = level * jnp.repeat(jnp.exp(steps), shape[axis_at] // shards_of).reshape((-1,) + (1,) * (len(shape) - 1 - axis_at))
    return level


def gaussian(stream_key, shape, width, limit, pieces=(), kind=jnp.bfloat16):
    drawn = jax.random.normal(stream_key, shape, jnp.float32) * width
    if len(pieces) > 0:
        drawn = steps_of(stream_key, shape, pieces, -0.22, 0.18) * drawn
    return jnp.clip(drawn, min=-limit, max=limit).astype(kind)


def setup_inputs(seed: int = 0) -> dict:
    streams_of = jax.random.split(jax.random.key(seed), 12)
    return {
        "residual": draw_residual(jax.random.fold_in(streams_of[11], 71), 0),
        "norm_gain": jnp.clip(1.0 + 0.18 * jax.random.normal(streams_of[1], (MODEL_WIDTH,), jnp.float32), 0.1, 1.9),
        "w_query": draw_w_query(jax.random.fold_in(streams_of[11], 71), 0),
        "w_key": draw_w_key(jax.random.fold_in(streams_of[11], 71), 0),
        "value_weight": gaussian(streams_of[4], (MODEL_WIDTH, KEY_VALUE_HEADS * HEAD_SIZE), MODEL_WIDTH ** -0.5, 0.0625, ((0, 16),)),
        "w_out": gaussian(streams_of[5], (QUERY_HEADS * HEAD_SIZE, MODEL_WIDTH), (QUERY_HEADS * HEAD_SIZE) ** -0.5, 0.0625, ((0, 16), (1, 16))),
        "decoder": gaussian(streams_of[6], (LATENTS, MODEL_WIDTH), 0.08, 0.5, ((0, 16), (1, 16))),
        "block_ids": draw_block_ids(jax.random.fold_in(streams_of[11], 71), 0),
        "latent_ids": draw_latent_ids(jax.random.fold_in(streams_of[11], 71), 0),
        "latent_vals": jnp.clip(jnp.exp(math.log(4.0) - 2.0794415 * jax.random.uniform(streams_of[9], (ROWS, TOPK), jnp.float32) ** steps_of(streams_of[9], (ROWS, TOPK), ((0, 16),), -0.2, 0.2)), 0.5, 4.0),
        "prompt_lens": draw_prompt_lens(jax.random.fold_in(streams_of[11], 71), 0),
    }


ROPE_BASE = 1000000.0
EPSILON = 1e-06
MASKED = -1e+30

def rope_tables(length, head_dim):
    frequency = ROPE_BASE ** (-(jnp.arange(head_dim // 2, dtype=jnp.float32) * 2.0) / head_dim)
    angles = jnp.arange(length, dtype=jnp.float32)[:, None] * frequency[None, :]
    angles = jnp.concatenate([angles, angles], axis=-1)
    return (jnp.cos(angles), jnp.sin(angles))

def apply_rotary(feature_map, cosine_table, sine_table):
    half_width = feature_map.shape[-1] // 2
    first_half = feature_map[..., :half_width]
    second_half = feature_map[..., half_width:]
    turned = jnp.concatenate([-second_half, first_half], axis=-1)
    return feature_map * cosine_table + turned * sine_table

def reference(residual, norm_gain, w_query, w_key, value_weight, w_out, decoder, block_ids, latent_ids, latent_vals, prompt_lens):
    row_total = residual.shape[0]
    row_grid = jnp.broadcast_to(jnp.arange(row_total, dtype=jnp.int32)[:, None], latent_ids.shape)
    ablated_list = []
    for number in range(ABLATION_STEPS):
        first_latent = (block_ids[number] * BLOCK).astype(jnp.int32)
        dec_block = lax.dynamic_slice_in_dim(decoder, first_latent, BLOCK, 0)
        offsets = (latent_ids - first_latent).astype(jnp.int32)
        inside = (offsets >= 0) & (offsets < BLOCK)
        coefs = jnp.zeros((row_total, BLOCK), jnp.float32)
        coefs = coefs.at[row_grid, jnp.where(inside, offsets, 0).astype(jnp.int32)].add(jnp.where(inside, latent_vals, jnp.zeros_like(latent_vals)))
        coefs = coefs.astype(jnp.bfloat16)
        removed = jnp.dot(coefs, dec_block, preferred_element_type=jnp.float32)
        ablated_list.append((residual.astype(jnp.float32) - removed).astype(jnp.bfloat16))
    ablated = jnp.stack(ablated_list)
    widened = ablated.astype(jnp.float32)
    mean_sq = lax.optimization_barrier(jnp.mean(widened * widened, axis=-1, keepdims=True))
    normed = (widened * lax.rsqrt(mean_sq + EPSILON) * norm_gain).astype(jnp.bfloat16)
    flattened = normed.reshape(ABLATION_STEPS * row_total, MODEL_WIDTH)
    query_vec = jnp.dot(flattened, w_query, preferred_element_type=jnp.float32)
    key_vector = jnp.dot(flattened, w_key, preferred_element_type=jnp.float32)
    value_vector = jnp.dot(flattened, value_weight, preferred_element_type=jnp.float32)
    prompt_row_count = row_total // PROMPT_ROWS
    cosine_table, sine_table = rope_tables(PROMPT_ROWS, HEAD_SIZE)
    query_vec = apply_rotary(query_vec.reshape(ABLATION_STEPS * prompt_row_count, PROMPT_ROWS, QUERY_HEADS, HEAD_SIZE), cosine_table[:, None, :], sine_table[:, None, :]).astype(jnp.bfloat16)
    key_vector = apply_rotary(key_vector.reshape(ABLATION_STEPS * prompt_row_count, PROMPT_ROWS, KEY_VALUE_HEADS, HEAD_SIZE), cosine_table[:, None, :], sine_table[:, None, :]).astype(jnp.bfloat16)
    value_vector = value_vector.reshape(ABLATION_STEPS * prompt_row_count, PROMPT_ROWS, KEY_VALUE_HEADS, HEAD_SIZE).astype(jnp.bfloat16)
    lengths = jnp.tile(prompt_lens, ABLATION_STEPS)
    query_group_size = QUERY_HEADS // KEY_VALUE_HEADS
    positions = jnp.arange(PROMPT_ROWS, dtype=jnp.int32)

    def attend(bundle):
        single_query, key_one, value_one, length = bundle
        query_expanded = single_query.astype(jnp.float32).reshape(PROMPT_ROWS, KEY_VALUE_HEADS, query_group_size, HEAD_SIZE)
        scores = jnp.einsum('qkgd,pkd->kgqp', query_expanded, key_one.astype(jnp.float32)) / math.sqrt(HEAD_SIZE)
        allowed = (positions[None, :] <= positions[:, None]) & (positions[None, :] < length)
        scores = jnp.where(allowed, scores, MASKED)
        weights = jax.nn.softmax(scores, axis=-1).astype(jnp.bfloat16)
        context = jnp.einsum('kgqp,pkd->qkgd', weights.astype(jnp.float32), value_one.astype(jnp.float32))
        return context.reshape(PROMPT_ROWS, QUERY_HEADS * HEAD_SIZE).astype(jnp.bfloat16)
    context = lax.map(attend, (query_vec, key_vector, value_vector, lengths))
    context = context.reshape(ABLATION_STEPS * row_total, N_TENSOR, QUERY_HEADS * HEAD_SIZE // N_TENSOR)
    out_groups = w_out.reshape(N_TENSOR, QUERY_HEADS * HEAD_SIZE // N_TENSOR, MODEL_WIDTH)

    def add_group(acc_total, grp_index):
        ctx_part = lax.dynamic_index_in_dim(context, grp_index, 1, keepdims=False)
        out_part = lax.dynamic_index_in_dim(out_groups, grp_index, 0, keepdims=False)
        partial_value = jnp.dot(ctx_part, out_part, preferred_element_type=jnp.float32)
        partial_value = lax.optimization_barrier(partial_value.astype(jnp.bfloat16)).astype(jnp.float32)
        return (acc_total + partial_value, None)
    summed, _ = lax.scan(add_group, jnp.zeros((ABLATION_STEPS * row_total, MODEL_WIDTH), jnp.float32), jnp.arange(N_TENSOR, dtype=jnp.int32))
    result = ablated.reshape(ABLATION_STEPS * row_total, MODEL_WIDTH).astype(jnp.float32) + summed
    return result.astype(jnp.bfloat16).reshape(ABLATION_STEPS, row_total, MODEL_WIDTH)
```

```python
import math

import jax
import jax.numpy as jnp
from jax import lax
from jax.sharding import PartitionSpec as P

QUERY_HEADS = 64
KEY_VALUE_HEADS = 8
HEAD_SIZE = 128
BLOCK = 128
PROMPT_ROWS = 256
ABLATION_STEPS = 2


ROPE_BASE = 1000000.0
EPSILON = 1e-06
MASKED = -1e30


def rope_tables(length, head_dim):
    frequency = ROPE_BASE ** (-(jnp.arange(head_dim // 2, dtype=jnp.float32) * 2.0) / head_dim)
    angles = jnp.arange(length, dtype=jnp.float32)[:, None] * frequency[None, :]
    angles = jnp.concatenate([angles, angles], axis=-1)
    return (jnp.cos(angles), jnp.sin(angles))


def apply_rotary(feature_map, cosine_table, sine_table):
    half_width = feature_map.shape[-1] // 2
    first_half = feature_map[..., :half_width]
    second_half = feature_map[..., half_width:]
    turned = jnp.concatenate([-second_half, first_half], axis=-1)
    return feature_map * cosine_table + turned * sine_table


def dense_codes(latent_ids, latent_vals, first_latent):
    offsets = latent_ids - first_latent
    columns = jnp.arange(BLOCK, dtype=jnp.int32)
    matched = offsets[:, :, None] == columns[None, None, :]
    picked = jnp.where(matched, latent_vals[:, :, None], jnp.zeros((), jnp.float32))
    return jnp.sum(picked, axis=1).astype(jnp.bfloat16)


def owner_rows(decoder, block_num):
    lat_count = decoder.shape[0]
    first_latent = block_num * BLOCK
    owner_dict = first_latent // lat_count
    row_offset = first_latent - owner_dict * lat_count
    return (lax.dynamic_slice_in_dim(decoder, row_offset, BLOCK, 0), owner_dict)


def fetch_blocks(decoder, block_ids):
    dict_pos = lax.axis_index("dict")
    dict_count = lax.axis_size("dict")
    blocks = []
    for number in range(ABLATION_STEPS):
        dec_rows, owner_dict = owner_rows(decoder, block_ids[number])
        blocks.append(jnp.where(dict_pos == owner_dict, dec_rows, jnp.zeros_like(dec_rows)))
    held = jnp.stack(blocks)
    step = 1
    while step < dict_count:
        pairs = [(i, i ^ step) for i in range(dict_count)]
        held = held + lax.ppermute(held, "dict", pairs)
        step *= 2
    return held


def body(
    residual,
    norm_gain,
    w_query,
    w_key,
    value_weight,
    w_out,
    decoder,
    block_ids,
    latent_ids,
    latent_vals,
    prompt_lens,
):
    row_count = residual.shape[0]
    col_count = residual.shape[1]
    tensor_pos = lax.axis_index("tensor")
    tensor_count = lax.axis_size("tensor")
    full_width = col_count * tensor_count
    coef_list = [
        dense_codes(latent_ids, latent_vals, block_ids[number] * BLOCK)
        for number in range(ABLATION_STEPS)
    ]
    col_list = []
    dec_blocks = fetch_blocks(decoder, block_ids)
    for number in range(ABLATION_STEPS):
        dec_slice = dec_blocks[number]
        removed = jnp.dot(coef_list[number], dec_slice, preferred_element_type=jnp.float32)
        col_list.append((residual.astype(jnp.float32) - removed).astype(jnp.bfloat16))
    own_cols = jnp.stack(col_list)
    ablated = lax.all_gather(own_cols, "tensor", axis=2, tiled=True)
    widened = ablated.astype(jnp.float32)
    mean_sq = jnp.mean(widened * widened, axis=-1, keepdims=True)
    normed = (widened * lax.rsqrt(mean_sq + EPSILON) * norm_gain).astype(jnp.bfloat16)
    normed = normed.reshape(ABLATION_STEPS * row_count, full_width)
    head_cols = w_query.shape[1]
    heads_dev = head_cols // HEAD_SIZE
    query_group_size = QUERY_HEADS // KEY_VALUE_HEADS
    kv_index = tensor_pos * heads_dev // query_group_size
    key_cols = lax.dynamic_slice_in_dim(w_key, kv_index * HEAD_SIZE, HEAD_SIZE, 1)
    value_cols = lax.dynamic_slice_in_dim(value_weight, kv_index * HEAD_SIZE, HEAD_SIZE, 1)
    packed = jnp.concatenate([w_query, key_cols, value_cols, w_out.T], axis=1)
    gathered = lax.all_gather(packed, "dict", axis=0, tiled=True)
    qkv_cols = head_cols + 2 * HEAD_SIZE
    qkv = jnp.dot(normed, gathered[:, :qkv_cols], preferred_element_type=jnp.float32)
    query_vec = qkv[:, :head_cols]
    key_vector = qkv[:, head_cols : head_cols + HEAD_SIZE]
    value_vector = qkv[:, head_cols + HEAD_SIZE : qkv_cols]
    prompt_count = row_count // PROMPT_ROWS
    cosine_table, sine_table = rope_tables(PROMPT_ROWS, HEAD_SIZE)
    query_vec = apply_rotary(
        query_vec.reshape(ABLATION_STEPS, prompt_count, PROMPT_ROWS, heads_dev, HEAD_SIZE),
        cosine_table[:, None, :],
        sine_table[:, None, :],
    ).astype(jnp.bfloat16)
    key_vector = apply_rotary(
        key_vector.reshape(ABLATION_STEPS, prompt_count, PROMPT_ROWS, HEAD_SIZE),
        cosine_table,
        sine_table,
    ).astype(jnp.bfloat16)
    value_vector = value_vector.reshape(
        ABLATION_STEPS, prompt_count, PROMPT_ROWS, HEAD_SIZE
    ).astype(jnp.bfloat16)
    positions = jnp.arange(PROMPT_ROWS, dtype=jnp.int32)
    scores = jnp.einsum(
        "spqhd,spkd->sphqk", query_vec, key_vector, preferred_element_type=jnp.float32
    ) / math.sqrt(HEAD_SIZE)
    allowed = (positions[None, None, :] <= positions[None, :, None]) & (
        positions[None, None, :] < prompt_lens[:, None, None]
    )
    scores = jnp.where(allowed[None, :, None, :, :], scores, MASKED)
    weights = jax.nn.softmax(scores, axis=-1).astype(jnp.bfloat16)
    context = jnp.einsum(
        "sphqk,spkd->spqhd", weights, value_vector, preferred_element_type=jnp.float32
    )
    context = context.astype(jnp.bfloat16).reshape(ABLATION_STEPS * row_count, head_cols)
    partial_value = lax.dot_general(
        context,
        gathered[:, qkv_cols:],
        (((1,), (1,)), ((), ())),
        preferred_element_type=jnp.float32,
    ).astype(jnp.bfloat16)
    summed = lax.psum_scatter(
        partial_value.astype(jnp.float32).astype(jnp.bfloat16),
        "tensor",
        scatter_dimension=1,
        tiled=True,
    ).astype(jnp.float32)
    result = own_cols.reshape(ABLATION_STEPS * row_count, col_count).astype(jnp.float32) + summed
    return result.astype(jnp.bfloat16).reshape(ABLATION_STEPS, row_count, col_count)


def solution(mesh):
    in_specs = (
        P("dict", "tensor"),
        P(),
        P("dict", "tensor"),
        P("dict", None),
        P("dict", None),
        P("tensor", "dict"),
        P("dict", "tensor"),
        P(),
        P("dict", None),
        P("dict", None),
        P("dict"),
    )
    out_specs = P(None, "dict", "tensor")
    return jax.shard_map(body, mesh=mesh, in_specs=in_specs, out_specs=out_specs, check_vma=False)
```

```python
import math

import jax
import jax.numpy as jnp
from jax import lax
from jax.sharding import PartitionSpec as P

QUERY_HEADS = 64
KEY_VALUE_HEADS = 8
HEAD_SIZE = 128
BLOCK = 128
PROMPT_ROWS = 256
ABLATION_STEPS = 2


ROPE_BASE = 1000000.0
EPSILON = 1e-06
MASKED = -1e30


def rope_tables(length, head_dim):
    frequency = ROPE_BASE ** (-(jnp.arange(head_dim // 2, dtype=jnp.float32) * 2.0) / head_dim)
    angles = jnp.arange(length, dtype=jnp.float32)[:, None] * frequency[None, :]
    angles = jnp.concatenate([angles, angles], axis=-1)
    return (jnp.cos(angles), jnp.sin(angles))


def apply_rotary(feature_map, cosine_table, sine_table):
    half_width = feature_map.shape[-1] // 2
    first_half = feature_map[..., :half_width]
    second_half = feature_map[..., half_width:]
    turned = jnp.concatenate([-second_half, first_half], axis=-1)
    return feature_map * cosine_table + turned * sine_table


def dense_codes(latent_ids, latent_vals, first_latent):
    offsets = latent_ids - first_latent
    columns = jnp.arange(BLOCK, dtype=jnp.int32)
    matched = offsets[:, :, None] == columns[None, None, :]
    picked = jnp.where(matched, latent_vals[:, :, None], jnp.zeros((), jnp.float32))
    return jnp.sum(picked, axis=1).astype(jnp.bfloat16)


def owner_rows(decoder, block_num):
    lat_count = decoder.shape[0]
    first_latent = block_num * BLOCK
    owner_dict = first_latent // lat_count
    row_offset = first_latent - owner_dict * lat_count
    return (lax.dynamic_slice_in_dim(decoder, row_offset, BLOCK, 0), owner_dict)


def fetch_blocks(decoder, block_ids):
    dict_pos = lax.axis_index("dict")
    dict_count = lax.axis_size("dict")
    blocks = []
    for number in range(ABLATION_STEPS):
        dec_rows, owner_dict = owner_rows(decoder, block_ids[number])
        blocks.append(jnp.where(dict_pos == owner_dict, dec_rows, jnp.zeros_like(dec_rows)))
    held = jnp.stack(blocks)
    step = 1
    while step < dict_count:
        pairs = [(i, i ^ step) for i in range(dict_count)]
        held = held + lax.ppermute(held, "dict", pairs)
        step *= 2
    return held


def gather_tensor(own, axis):
    count = lax.axis_size("tensor")
    inner = 4 if count % 4 == 0 else 1
    outer = count // inner
    pos = lax.axis_index("tensor")
    hi = pos // inner
    lo = pos % inner
    grid = []
    for d_hi in range(outer):
        row = []
        for d_lo in range(inner):
            if d_hi == 0 and d_lo == 0:
                row.append(own)
                continue
            pairs = []
            for src_pos in range(count):
                dst_hi = (src_pos // inner - d_hi) % outer
                dst_lo = (src_pos % inner - d_lo) % inner
                pairs.append((src_pos, dst_hi * inner + dst_lo))
            row.append(lax.ppermute(own, "tensor", pairs))
        grid.append(jnp.stack(row))
    grid = jnp.stack(grid)
    grid = jnp.roll(grid, hi, axis=0)
    grid = jnp.roll(grid, lo, axis=1)
    grid = grid.reshape((count,) + own.shape)
    return jnp.concatenate([grid[j] for j in range(count)], axis=axis)


def body(
    residual,
    norm_gain,
    w_query,
    w_key,
    value_weight,
    w_out,
    decoder,
    block_ids,
    latent_ids,
    latent_vals,
    prompt_lens,
):
    row_count = residual.shape[0]
    col_count = residual.shape[1]
    tensor_pos = lax.axis_index("tensor")
    tensor_count = lax.axis_size("tensor")
    full_width = col_count * tensor_count
    coef_list = [
        dense_codes(latent_ids, latent_vals, block_ids[number] * BLOCK)
        for number in range(ABLATION_STEPS)
    ]
    col_list = []
    dec_blocks = fetch_blocks(decoder, block_ids)
    for number in range(ABLATION_STEPS):
        dec_slice = dec_blocks[number]
        removed = jnp.dot(coef_list[number], dec_slice, preferred_element_type=jnp.float32)
        col_list.append((residual.astype(jnp.float32) - removed).astype(jnp.bfloat16))
    own_cols = jnp.stack(col_list)
    ablated = gather_tensor(own_cols, 2)
    widened = ablated.astype(jnp.float32)
    mean_sq = jnp.mean(widened * widened, axis=-1, keepdims=True)
    normed = (widened * lax.rsqrt(mean_sq + EPSILON) * norm_gain).astype(jnp.bfloat16)
    normed = normed.reshape(ABLATION_STEPS * row_count, full_width)
    head_cols = w_query.shape[1]
    heads_dev = head_cols // HEAD_SIZE
    query_group_size = QUERY_HEADS // KEY_VALUE_HEADS
    kv_index = tensor_pos * heads_dev // query_group_size
    key_cols = lax.dynamic_slice_in_dim(w_key, kv_index * HEAD_SIZE, HEAD_SIZE, 1)
    value_cols = lax.dynamic_slice_in_dim(value_weight, kv_index * HEAD_SIZE, HEAD_SIZE, 1)
    packed = jnp.concatenate([w_query, key_cols, value_cols, w_out.T], axis=1)
    gathered = lax.all_gather(packed, "dict", axis=0, tiled=True)
    qkv_cols = head_cols + 2 * HEAD_SIZE
    qkv = jnp.dot(normed, gathered[:, :qkv_cols], preferred_element_type=jnp.float32)
    query_vec = qkv[:, :head_cols]
    key_vector = qkv[:, head_cols : head_cols + HEAD_SIZE]
    value_vector = qkv[:, head_cols + HEAD_SIZE : qkv_cols]
    prompt_count = row_count // PROMPT_ROWS
    cosine_table, sine_table = rope_tables(PROMPT_ROWS, HEAD_SIZE)
    query_vec = apply_rotary(
        query_vec.reshape(ABLATION_STEPS, prompt_count, PROMPT_ROWS, heads_dev, HEAD_SIZE),
        cosine_table[:, None, :],
        sine_table[:, None, :],
    ).astype(jnp.bfloat16)
    key_vector = apply_rotary(
        key_vector.reshape(ABLATION_STEPS, prompt_count, PROMPT_ROWS, HEAD_SIZE),
        cosine_table,
        sine_table,
    ).astype(jnp.bfloat16)
    value_vector = value_vector.reshape(
        ABLATION_STEPS, prompt_count, PROMPT_ROWS, HEAD_SIZE
    ).astype(jnp.bfloat16)
    positions = jnp.arange(PROMPT_ROWS, dtype=jnp.int32)
    scores = jnp.einsum(
        "spqhd,spkd->sphqk", query_vec, key_vector, preferred_element_type=jnp.float32
    ) / math.sqrt(HEAD_SIZE)
    allowed = (positions[None, None, :] <= positions[None, :, None]) & (
        positions[None, None, :] < prompt_lens[:, None, None]
    )
    scores = jnp.where(allowed[None, :, None, :, :], scores, MASKED)
    weights = jax.nn.softmax(scores, axis=-1).astype(jnp.bfloat16)
    context = jnp.einsum(
        "sphqk,spkd->spqhd", weights, value_vector, preferred_element_type=jnp.float32
    )
    context = context.astype(jnp.bfloat16).reshape(ABLATION_STEPS * row_count, head_cols)
    partial_value = lax.dot_general(
        context,
        gathered[:, qkv_cols:],
        (((1,), (1,)), ((), ())),
        preferred_element_type=jnp.float32,
    ).astype(jnp.bfloat16)
    summed = lax.psum_scatter(
        partial_value.astype(jnp.float32).astype(jnp.bfloat16),
        "tensor",
        scatter_dimension=1,
        tiled=True,
    ).astype(jnp.float32)
    result = own_cols.reshape(ABLATION_STEPS * row_count, col_count).astype(jnp.float32) + summed
    return result.astype(jnp.bfloat16).reshape(ABLATION_STEPS, row_count, col_count)


def solution(mesh):
    in_specs = (
        P("dict", "tensor"),
        P(),
        P("dict", "tensor"),
        P("dict", None),
        P("dict", None),
        P("tensor", "dict"),
        P("dict", "tensor"),
        P(),
        P("dict", None),
        P("dict", None),
        P("dict"),
    )
    out_specs = P(None, "dict", "tensor")
    return jax.shard_map(body, mesh=mesh, in_specs=in_specs, out_specs=out_specs, check_vma=False)
```

```python
import math

import jax
import jax.numpy as jnp
from jax import lax
from jax.sharding import PartitionSpec as P

QUERY_HEADS = 64
KEY_VALUE_HEADS = 8
HEAD_SIZE = 128
BLOCK = 128
PROMPT_ROWS = 256
ABLATION_STEPS = 2


ROPE_BASE = 1000000.0
EPSILON = 1e-06
MASKED = -1e30


def rope_tables(length, head_dim):
    frequency = ROPE_BASE ** (-(jnp.arange(head_dim // 2, dtype=jnp.float32) * 2.0) / head_dim)
    angles = jnp.arange(length, dtype=jnp.float32)[:, None] * frequency[None, :]
    angles = jnp.concatenate([angles, angles], axis=-1)
    return (jnp.cos(angles), jnp.sin(angles))


def apply_rotary(feature_map, cosine_table, sine_table):
    half_width = feature_map.shape[-1] // 2
    first_half = feature_map[..., :half_width]
    second_half = feature_map[..., half_width:]
    turned = jnp.concatenate([-second_half, first_half], axis=-1)
    return feature_map * cosine_table + turned * sine_table


def dense_codes(latent_ids, latent_vals, first_latent):
    offsets = latent_ids - first_latent
    columns = jnp.arange(BLOCK, dtype=jnp.int32)
    matched = offsets[:, :, None] == columns[None, None, :]
    picked = jnp.where(matched, latent_vals[:, :, None], jnp.zeros((), jnp.float32))
    return jnp.sum(picked, axis=1).astype(jnp.bfloat16)


def owner_rows(decoder, block_num):
    lat_count = decoder.shape[0]
    first_latent = block_num * BLOCK
    owner_dict = first_latent // lat_count
    row_offset = first_latent - owner_dict * lat_count
    return (lax.dynamic_slice_in_dim(decoder, row_offset, BLOCK, 0), owner_dict)


def fetch_blocks(decoder, block_ids):
    dict_pos = lax.axis_index("dict")
    dict_count = lax.axis_size("dict")
    blocks = []
    for number in range(ABLATION_STEPS):
        dec_rows, owner_dict = owner_rows(decoder, block_ids[number])
        blocks.append(jnp.where(dict_pos == owner_dict, dec_rows, jnp.zeros_like(dec_rows)))
    held = jnp.stack(blocks)
    step = 1
    while step < dict_count:
        pairs = [(i, i ^ step) for i in range(dict_count)]
        held = held + lax.ppermute(held, "dict", pairs)
        step *= 2
    return held


def body(
    residual,
    norm_gain,
    w_query,
    w_key,
    value_weight,
    w_out,
    decoder,
    block_ids,
    latent_ids,
    latent_vals,
    prompt_lens,
):
    row_count = residual.shape[0]
    col_count = residual.shape[1]
    tensor_pos = lax.axis_index("tensor")
    tensor_count = lax.axis_size("tensor")
    full_width = col_count * tensor_count
    head_cols = w_query.shape[1]
    heads_dev = head_cols // HEAD_SIZE
    query_group_size = QUERY_HEADS // KEY_VALUE_HEADS
    kv_index = tensor_pos * heads_dev // query_group_size
    assert 2 * heads_dev <= query_group_size
    is_key_side = tensor_pos % 2 == 0
    key_cols = lax.dynamic_slice_in_dim(w_key, kv_index * HEAD_SIZE, HEAD_SIZE, 1)
    value_cols = lax.dynamic_slice_in_dim(value_weight, kv_index * HEAD_SIZE, HEAD_SIZE, 1)
    kv_cols = jnp.where(is_key_side, key_cols, value_cols)
    packed = jnp.concatenate([w_query, kv_cols, w_out.T], axis=1)
    gathered = lax.all_gather(packed, "dict", axis=0, tiled=True)
    coef_list = [
        dense_codes(latent_ids, latent_vals, block_ids[number] * BLOCK)
        for number in range(ABLATION_STEPS)
    ]
    col_list = []
    dec_blocks = fetch_blocks(decoder, block_ids)
    for number in range(ABLATION_STEPS):
        dec_slice = dec_blocks[number]
        removed = jnp.dot(coef_list[number], dec_slice, preferred_element_type=jnp.float32)
        col_list.append((residual.astype(jnp.float32) - removed).astype(jnp.bfloat16))
    own_cols = jnp.stack(col_list)
    own_cols, gathered = lax.optimization_barrier((own_cols, gathered))
    ablated = lax.all_gather(own_cols, "tensor", axis=2, tiled=True)
    widened = ablated.astype(jnp.float32)
    mean_sq = jnp.mean(widened * widened, axis=-1, keepdims=True)
    normed = (widened * lax.rsqrt(mean_sq + EPSILON) * norm_gain).astype(jnp.bfloat16)
    normed = normed.reshape(ABLATION_STEPS * row_count, full_width)
    qkv_cols = head_cols + HEAD_SIZE
    qkv = jnp.dot(normed, gathered[:, :qkv_cols], preferred_element_type=jnp.float32)
    query_vec = qkv[:, :head_cols]
    kv_vector = qkv[:, head_cols:qkv_cols]
    prompt_count = row_count // PROMPT_ROWS
    cosine_table, sine_table = rope_tables(PROMPT_ROWS, HEAD_SIZE)
    query_vec = apply_rotary(
        query_vec.reshape(ABLATION_STEPS, prompt_count, PROMPT_ROWS, heads_dev, HEAD_SIZE),
        cosine_table[:, None, :],
        sine_table[:, None, :],
    ).astype(jnp.bfloat16)
    kv_vector = kv_vector.reshape(ABLATION_STEPS, prompt_count, PROMPT_ROWS, HEAD_SIZE)
    kv_rotated = apply_rotary(kv_vector, cosine_table, sine_table)
    own_kv = jnp.where(is_key_side, kv_rotated, kv_vector).astype(jnp.bfloat16)
    tensor_pairs = [(i, i ^ 1) for i in range(tensor_count)]
    other_kv = lax.ppermute(own_kv, "tensor", tensor_pairs)
    key_vector = jnp.where(is_key_side, own_kv, other_kv)
    value_vector = jnp.where(is_key_side, other_kv, own_kv)
    positions = jnp.arange(PROMPT_ROWS, dtype=jnp.int32)
    scores = jnp.einsum(
        "spqhd,spkd->sphqk", query_vec, key_vector, preferred_element_type=jnp.float32
    ) / math.sqrt(HEAD_SIZE)
    allowed = (positions[None, None, :] <= positions[None, :, None]) & (
        positions[None, None, :] < prompt_lens[:, None, None]
    )
    scores = jnp.where(allowed[None, :, None, :, :], scores, MASKED)
    weights = jax.nn.softmax(scores, axis=-1).astype(jnp.bfloat16)
    context = jnp.einsum(
        "sphqk,spkd->spqhd", weights, value_vector, preferred_element_type=jnp.float32
    )
    context = context.astype(jnp.bfloat16).reshape(ABLATION_STEPS * row_count, head_cols)
    partial_value = lax.dot_general(
        context,
        gathered[:, qkv_cols:],
        (((1,), (1,)), ((), ())),
        preferred_element_type=jnp.float32,
    ).astype(jnp.bfloat16)
    summed = lax.psum_scatter(
        partial_value.astype(jnp.float32).astype(jnp.bfloat16),
        "tensor",
        scatter_dimension=1,
        tiled=True,
    ).astype(jnp.float32)
    result = own_cols.reshape(ABLATION_STEPS * row_count, col_count).astype(jnp.float32) + summed
    return result.astype(jnp.bfloat16).reshape(ABLATION_STEPS, row_count, col_count)


def solution(mesh):
    in_specs = (
        P("dict", "tensor"),
        P(),
        P("dict", "tensor"),
        P("dict", None),
        P("dict", None),
        P("tensor", "dict"),
        P("dict", "tensor"),
        P(),
        P("dict", None),
        P("dict", None),
        P("dict"),
    )
    out_specs = P(None, "dict", "tensor")
    return jax.shard_map(body, mesh=mesh, in_specs=in_specs, out_specs=out_specs, check_vma=False)
```

```python
import math

import jax
import jax.numpy as jnp
from jax import lax
from jax.sharding import PartitionSpec as P

QUERY_HEADS = 64
KEY_VALUE_HEADS = 8
HEAD_SIZE = 128
BLOCK = 128
PROMPT_ROWS = 256
ABLATION_STEPS = 2


ROPE_BASE = 1000000.0
EPSILON = 1e-06
MASKED = -1e30


def rope_tables(length, head_dim):
    frequency = ROPE_BASE ** (-(jnp.arange(head_dim // 2, dtype=jnp.float32) * 2.0) / head_dim)
    angles = jnp.arange(length, dtype=jnp.float32)[:, None] * frequency[None, :]
    angles = jnp.concatenate([angles, angles], axis=-1)
    return (jnp.cos(angles), jnp.sin(angles))


def apply_rotary(feature_map, cosine_table, sine_table):
    half_width = feature_map.shape[-1] // 2
    first_half = feature_map[..., :half_width]
    second_half = feature_map[..., half_width:]
    turned = jnp.concatenate([-second_half, first_half], axis=-1)
    return feature_map * cosine_table + turned * sine_table


def dense_codes(latent_ids, latent_vals, first_latent):
    offsets = latent_ids - first_latent
    columns = jnp.arange(BLOCK, dtype=jnp.int32)
    matched = offsets[:, :, None] == columns[None, None, :]
    picked = jnp.where(matched, latent_vals[:, :, None], jnp.zeros((), jnp.float32))
    return jnp.sum(picked, axis=1).astype(jnp.bfloat16)


def owner_rows(decoder, block_num):
    lat_count = decoder.shape[0]
    first_latent = block_num * BLOCK
    owner_dict = first_latent // lat_count
    row_offset = first_latent - owner_dict * lat_count
    return (lax.dynamic_slice_in_dim(decoder, row_offset, BLOCK, 0), owner_dict)


DICT = ("dict_hi", "core")


def dict_index():
    return lax.axis_index("dict_hi") * lax.axis_size("core") + lax.axis_index("core")


def dict_size():
    return lax.axis_size("dict_hi") * lax.axis_size("core")


def butterfly_sum(value, axis, count):
    step = 1
    while step < count:
        pairs = [(i, i ^ step) for i in range(count)]
        value = value + lax.ppermute(value, axis, pairs)
        step *= 2
    return value


def fetch_blocks(decoder, block_ids):
    dict_pos = dict_index()
    dict_count = dict_size()
    blocks = []
    for number in range(ABLATION_STEPS):
        dec_rows, owner_dict = owner_rows(decoder, block_ids[number])
        blocks.append(jnp.where(dict_pos == owner_dict, dec_rows, jnp.zeros_like(dec_rows)))
    held = jnp.stack(blocks)
    step = 1
    while step < dict_count:
        pairs = [(i, i ^ step) for i in range(dict_count)]
        held = held + lax.ppermute(held, DICT, pairs)
        step *= 2
    return held


def body(
    residual,
    norm_gain,
    w_query,
    w_key,
    value_weight,
    w_out,
    decoder,
    block_ids,
    latent_ids,
    latent_vals,
    prompt_lens,
):
    row_count = residual.shape[0]
    col_count = residual.shape[1]
    tensor_pos = lax.axis_index("tensor")
    tensor_count = lax.axis_size("tensor")
    full_width = col_count * tensor_count
    head_cols = w_query.shape[1]
    heads_dev = head_cols // HEAD_SIZE
    query_group_size = QUERY_HEADS // KEY_VALUE_HEADS
    kv_index = tensor_pos * heads_dev // query_group_size
    assert 2 * heads_dev <= query_group_size
    is_key_side = tensor_pos % 2 == 0
    key_cols = lax.dynamic_slice_in_dim(w_key, kv_index * HEAD_SIZE, HEAD_SIZE, 1)
    value_cols = lax.dynamic_slice_in_dim(value_weight, kv_index * HEAD_SIZE, HEAD_SIZE, 1)
    kv_cols = jnp.where(is_key_side, key_cols, value_cols)
    packed = jnp.concatenate([w_query, kv_cols, w_out.T], axis=1)
    own_half = lax.all_gather(packed, "dict_hi", axis=0, tiled=False)
    coef_list = [
        dense_codes(latent_ids, latent_vals, block_ids[number] * BLOCK)
        for number in range(ABLATION_STEPS)
    ]
    col_list = []
    dec_blocks = fetch_blocks(decoder, block_ids)
    for number in range(ABLATION_STEPS):
        dec_slice = dec_blocks[number]
        removed = jnp.dot(coef_list[number], dec_slice, preferred_element_type=jnp.float32)
        col_list.append((residual.astype(jnp.float32) - removed).astype(jnp.bfloat16))
    own_cols = jnp.stack(col_list)
    widened = own_cols.astype(jnp.float32)
    sum_sq = butterfly_sum(jnp.sum(widened * widened, axis=-1, keepdims=True), "tensor", tensor_count)
    mean_sq = sum_sq / full_width
    gain_cols = lax.dynamic_slice_in_dim(norm_gain, tensor_pos * col_count, col_count)
    normed_cols = (widened * lax.rsqrt(mean_sq + EPSILON) * gain_cols).astype(jnp.bfloat16)
    normed_cols, own_half = lax.optimization_barrier((normed_cols, own_half))
    core_count = lax.axis_size("core")
    core_pos = lax.axis_index("core")
    halves = [own_half]
    for shift in range(1, core_count):
        core_pairs = [(i, (i + shift) % core_count) for i in range(core_count)]
        halves.append(lax.ppermute(own_half, "core", core_pairs))
    ordered = []
    for core_id in range(core_count):
        pick = halves[0]
        for k in range(1, core_count):
            pick = jnp.where((core_pos - k) % core_count == core_id, halves[k], pick)
        ordered.append(pick)
    gathered = jnp.stack(ordered, axis=1).reshape(-1, packed.shape[1])
    normed = lax.all_gather(normed_cols, "tensor", axis=2, tiled=True)
    normed = normed.reshape(ABLATION_STEPS * row_count, full_width)
    qkv_cols = head_cols + HEAD_SIZE
    qkv = jnp.dot(normed, gathered[:, :qkv_cols], preferred_element_type=jnp.float32)
    query_vec = qkv[:, :head_cols]
    kv_vector = qkv[:, head_cols:qkv_cols]
    prompt_count = row_count // PROMPT_ROWS
    cosine_table, sine_table = rope_tables(PROMPT_ROWS, HEAD_SIZE)
    query_vec = apply_rotary(
        query_vec.reshape(ABLATION_STEPS, prompt_count, PROMPT_ROWS, heads_dev, HEAD_SIZE),
        cosine_table[:, None, :],
        sine_table[:, None, :],
    ).astype(jnp.bfloat16)
    kv_vector = kv_vector.reshape(ABLATION_STEPS, prompt_count, PROMPT_ROWS, HEAD_SIZE)
    kv_rotated = apply_rotary(kv_vector, cosine_table, sine_table)
    own_kv = jnp.where(is_key_side, kv_rotated, kv_vector).astype(jnp.bfloat16)
    tensor_pairs = [(i, i ^ 1) for i in range(tensor_count)]
    other_kv = lax.ppermute(own_kv, "tensor", tensor_pairs)
    key_vector = jnp.where(is_key_side, own_kv, other_kv)
    value_vector = jnp.where(is_key_side, other_kv, own_kv)
    positions = jnp.arange(PROMPT_ROWS, dtype=jnp.int32)
    scores = jnp.einsum(
        "spqhd,spkd->sphqk", query_vec, key_vector, preferred_element_type=jnp.float32
    ) / math.sqrt(HEAD_SIZE)
    allowed = (positions[None, None, :] <= positions[None, :, None]) & (
        positions[None, None, :] < prompt_lens[:, None, None]
    )
    scores = jnp.where(allowed[None, :, None, :, :], scores, MASKED)
    weights = jax.nn.softmax(scores, axis=-1).astype(jnp.bfloat16)
    context = jnp.einsum(
        "sphqk,spkd->spqhd", weights, value_vector, preferred_element_type=jnp.float32
    )
    context = context.astype(jnp.bfloat16).reshape(ABLATION_STEPS * row_count, head_cols)
    partial_value = lax.dot_general(
        context,
        gathered[:, qkv_cols:],
        (((1,), (1,)), ((), ())),
        preferred_element_type=jnp.float32,
    ).astype(jnp.bfloat16)
    summed = lax.psum_scatter(
        partial_value.astype(jnp.float32).astype(jnp.bfloat16),
        "tensor",
        scatter_dimension=1,
        tiled=True,
    ).astype(jnp.float32)
    result = own_cols.reshape(ABLATION_STEPS * row_count, col_count).astype(jnp.float32) + summed
    return result.astype(jnp.bfloat16).reshape(ABLATION_STEPS, row_count, col_count)


def solution(mesh):
    dict_count = mesh.shape["dict"]
    core_count = 2 if dict_count % 2 == 0 else 1
    devices = mesh.devices.reshape(dict_count // core_count, core_count, mesh.shape["tensor"])
    fine = jax.sharding.Mesh(devices, ("dict_hi", "core", "tensor"))
    in_specs = (
        P(DICT, "tensor"),
        P(),
        P(DICT, "tensor"),
        P(DICT, None),
        P(DICT, None),
        P("tensor", DICT),
        P(DICT, "tensor"),
        P(),
        P(DICT, None),
        P(DICT, None),
        P(DICT),
    )
    out_specs = P(None, DICT, "tensor")
    return jax.shard_map(body, mesh=fine, in_specs=in_specs, out_specs=out_specs, check_vma=False)
```

```python
import math

import jax
import jax.numpy as jnp
from jax import lax
from jax.sharding import PartitionSpec as P

QUERY_HEADS = 64
KEY_VALUE_HEADS = 8
HEAD_SIZE = 128
BLOCK = 128
PROMPT_ROWS = 256
ABLATION_STEPS = 2


ROPE_BASE = 1000000.0
EPSILON = 1e-06
MASKED = -1e30


def rope_tables(length, head_dim):
    frequency = ROPE_BASE ** (-(jnp.arange(head_dim // 2, dtype=jnp.float32) * 2.0) / head_dim)
    angles = jnp.arange(length, dtype=jnp.float32)[:, None] * frequency[None, :]
    angles = jnp.concatenate([angles, angles], axis=-1)
    return (jnp.cos(angles), jnp.sin(angles))


def apply_rotary(feature_map, cosine_table, sine_table):
    half_width = feature_map.shape[-1] // 2
    first_half = feature_map[..., :half_width]
    second_half = feature_map[..., half_width:]
    turned = jnp.concatenate([-second_half, first_half], axis=-1)
    return feature_map * cosine_table + turned * sine_table


def dense_codes(latent_ids, latent_vals, first_latent):
    offsets = latent_ids - first_latent
    columns = jnp.arange(BLOCK, dtype=jnp.int32)
    matched = offsets[:, :, None] == columns[None, None, :]
    picked = jnp.where(matched, latent_vals[:, :, None], jnp.zeros((), jnp.float32))
    return jnp.sum(picked, axis=1).astype(jnp.bfloat16)


def owner_rows(decoder, block_num):
    lat_count = decoder.shape[0]
    first_latent = block_num * BLOCK
    owner_dict = first_latent // lat_count
    row_offset = first_latent - owner_dict * lat_count
    return (lax.dynamic_slice_in_dim(decoder, row_offset, BLOCK, 0), owner_dict)


DICT = ("dict_hi", "core")


def dict_index():
    return lax.axis_index("dict_hi") * lax.axis_size("core") + lax.axis_index("core")


def dict_size():
    return lax.axis_size("dict_hi") * lax.axis_size("core")


def butterfly_sum(value, axis, count):
    step = 1
    while step < count:
        pairs = [(i, i ^ step) for i in range(count)]
        value = value + lax.ppermute(value, axis, pairs)
        step *= 2
    return value


def fetch_blocks(decoder, block_ids):
    dict_pos = dict_index()
    dict_count = dict_size()
    blocks = []
    for number in range(ABLATION_STEPS):
        dec_rows, owner_dict = owner_rows(decoder, block_ids[number])
        blocks.append(jnp.where(dict_pos == owner_dict, dec_rows, jnp.zeros_like(dec_rows)))
    held = jnp.stack(blocks)
    step = 1
    while step < dict_count:
        pairs = [(i, i ^ step) for i in range(dict_count)]
        held = held + lax.ppermute(held, DICT, pairs)
        step *= 2
    return held


def body(
    residual,
    norm_gain,
    w_query,
    w_key,
    value_weight,
    w_out,
    decoder,
    block_ids,
    latent_ids,
    latent_vals,
    prompt_lens,
):
    row_count = residual.shape[0]
    col_count = residual.shape[1]
    tensor_pos = lax.axis_index("tensor")
    tensor_count = lax.axis_size("tensor")
    full_width = col_count * tensor_count
    head_cols = w_query.shape[1]
    heads_dev = head_cols // HEAD_SIZE
    query_group_size = QUERY_HEADS // KEY_VALUE_HEADS
    kv_index = tensor_pos * heads_dev // query_group_size
    assert 2 * heads_dev <= query_group_size
    is_key_side = tensor_pos % 2 == 0
    key_cols = lax.dynamic_slice_in_dim(w_key, kv_index * HEAD_SIZE, HEAD_SIZE, 1)
    value_cols = lax.dynamic_slice_in_dim(value_weight, kv_index * HEAD_SIZE, HEAD_SIZE, 1)
    kv_cols = jnp.where(is_key_side, key_cols, value_cols)
    packed = jnp.concatenate([w_query, kv_cols, w_out.T], axis=1)
    gathered = lax.all_gather(packed, DICT, axis=0, tiled=True)
    coef_list = [
        dense_codes(latent_ids, latent_vals, block_ids[number] * BLOCK)
        for number in range(ABLATION_STEPS)
    ]
    col_list = []
    dec_blocks = fetch_blocks(decoder, block_ids)
    for number in range(ABLATION_STEPS):
        dec_slice = dec_blocks[number]
        removed = jnp.dot(coef_list[number], dec_slice, preferred_element_type=jnp.float32)
        col_list.append((residual.astype(jnp.float32) - removed).astype(jnp.bfloat16))
    own_cols = jnp.stack(col_list)
    widened = own_cols.astype(jnp.float32)
    sum_sq = butterfly_sum(jnp.sum(widened * widened, axis=-1, keepdims=True), "tensor", tensor_count)
    mean_sq = sum_sq / full_width
    gain_cols = lax.dynamic_slice_in_dim(norm_gain, tensor_pos * col_count, col_count)
    normed_cols = (widened * lax.rsqrt(mean_sq + EPSILON) * gain_cols).astype(jnp.bfloat16)
    normed_cols, gathered = lax.optimization_barrier((normed_cols, gathered))
    normed = lax.all_gather(normed_cols, "tensor", axis=2, tiled=True)
    normed = normed.reshape(ABLATION_STEPS * row_count, full_width)
    qkv_cols = head_cols + HEAD_SIZE
    qkv = jnp.dot(normed, gathered[:, :qkv_cols], preferred_element_type=jnp.float32)
    query_vec = qkv[:, :head_cols]
    kv_vector = qkv[:, head_cols:qkv_cols]
    prompt_count = row_count // PROMPT_ROWS
    cosine_table, sine_table = rope_tables(PROMPT_ROWS, HEAD_SIZE)
    query_vec = apply_rotary(
        query_vec.reshape(ABLATION_STEPS, prompt_count, PROMPT_ROWS, heads_dev, HEAD_SIZE),
        cosine_table[:, None, :],
        sine_table[:, None, :],
    ).astype(jnp.bfloat16)
    kv_vector = kv_vector.reshape(ABLATION_STEPS, prompt_count, PROMPT_ROWS, HEAD_SIZE)
    kv_rotated = apply_rotary(kv_vector, cosine_table, sine_table)
    own_kv = jnp.where(is_key_side, kv_rotated, kv_vector).astype(jnp.bfloat16)
    tensor_pairs = [(i, i ^ 1) for i in range(tensor_count)]
    other_kv = lax.ppermute(own_kv, "tensor", tensor_pairs)
    key_vector = jnp.where(is_key_side, own_kv, other_kv)
    value_vector = jnp.where(is_key_side, other_kv, own_kv)
    positions = jnp.arange(PROMPT_ROWS, dtype=jnp.int32)
    scores = jnp.einsum(
        "spqhd,spkd->sphqk", query_vec, key_vector, preferred_element_type=jnp.float32
    ) / math.sqrt(HEAD_SIZE)
    allowed = (positions[None, None, :] <= positions[None, :, None]) & (
        positions[None, None, :] < prompt_lens[:, None, None]
    )
    scores = jnp.where(allowed[None, :, None, :, :], scores, MASKED)
    weights = jax.nn.softmax(scores, axis=-1).astype(jnp.bfloat16)
    context = jnp.einsum(
        "sphqk,spkd->spqhd", weights, value_vector, preferred_element_type=jnp.float32
    )
    context = context.astype(jnp.bfloat16).reshape(ABLATION_STEPS * row_count, head_cols)
    partial_value = lax.dot_general(
        context,
        gathered[:, qkv_cols:],
        (((1,), (1,)), ((), ())),
        preferred_element_type=jnp.float32,
    ).astype(jnp.bfloat16)
    summed = lax.psum_scatter(
        partial_value.astype(jnp.float32).astype(jnp.bfloat16),
        "tensor",
        scatter_dimension=1,
        tiled=True,
    ).astype(jnp.float32)
    result = own_cols.reshape(ABLATION_STEPS * row_count, col_count).astype(jnp.float32) + summed
    return result.astype(jnp.bfloat16).reshape(ABLATION_STEPS, row_count, col_count)


def solution(mesh):
    dict_count = mesh.shape["dict"]
    core_count = 2 if dict_count % 2 == 0 else 1
    devices = mesh.devices.reshape(dict_count // core_count, core_count, mesh.shape["tensor"])
    fine = jax.sharding.Mesh(devices, ("dict_hi", "core", "tensor"))
    in_specs = (
        P(DICT, "tensor"),
        P(),
        P(DICT, "tensor"),
        P(DICT, None),
        P(DICT, None),
        P("tensor", DICT),
        P(DICT, "tensor"),
        P(),
        P(DICT, None),
        P(DICT, None),
        P(DICT),
    )
    out_specs = P(None, DICT, "tensor")
    return jax.shard_map(body, mesh=fine, in_specs=in_specs, out_specs=out_specs, check_vma=False)
```

```python
import math

import jax
import jax.numpy as jnp
from jax import lax
from jax.sharding import PartitionSpec as P

QUERY_HEADS = 64
KEY_VALUE_HEADS = 8
HEAD_SIZE = 128
BLOCK = 128
PROMPT_ROWS = 256
ABLATION_STEPS = 2


ROPE_BASE = 1000000.0
EPSILON = 1e-06
MASKED = -1e30


def rope_tables(length, head_dim):
    frequency = ROPE_BASE ** (-(jnp.arange(head_dim // 2, dtype=jnp.float32) * 2.0) / head_dim)
    angles = jnp.arange(length, dtype=jnp.float32)[:, None] * frequency[None, :]
    angles = jnp.concatenate([angles, angles], axis=-1)
    return (jnp.cos(angles), jnp.sin(angles))


def apply_rotary(feature_map, cosine_table, sine_table):
    half_width = feature_map.shape[-1] // 2
    first_half = feature_map[..., :half_width]
    second_half = feature_map[..., half_width:]
    turned = jnp.concatenate([-second_half, first_half], axis=-1)
    return feature_map * cosine_table + turned * sine_table


def dense_codes(latent_ids, latent_vals, first_latent):
    offsets = latent_ids - first_latent
    columns = jnp.arange(BLOCK, dtype=jnp.int32)
    matched = offsets[:, :, None] == columns[None, None, :]
    picked = jnp.where(matched, latent_vals[:, :, None], jnp.zeros((), jnp.float32))
    return jnp.sum(picked, axis=1).astype(jnp.bfloat16)


def owner_rows(decoder, block_num):
    lat_count = decoder.shape[0]
    first_latent = block_num * BLOCK
    owner_dict = first_latent // lat_count
    row_offset = first_latent - owner_dict * lat_count
    return (lax.dynamic_slice_in_dim(decoder, row_offset, BLOCK, 0), owner_dict)


DICT = ("dict_hi", "core")


def dict_index():
    return lax.axis_index("dict_hi") * lax.axis_size("core") + lax.axis_index("core")


def dict_size():
    return lax.axis_size("dict_hi") * lax.axis_size("core")


def butterfly_sum(value, axis, count):
    step = 1
    while step < count:
        pairs = [(i, i ^ step) for i in range(count)]
        value = value + lax.ppermute(value, axis, pairs)
        step *= 2
    return value


def ring_gather_dict(block):
    count = dict_size()
    cores = lax.axis_size("core")
    hi = lax.axis_size("dict_hi")
    lanes = 2 if hi % 2 == 0 else 1
    along = hi // lanes
    chips = [(x, 0) for x in range(along)]
    if lanes == 2:
        chips += [(x, 1) for x in reversed(range(along))]
    ring = [(x * lanes + z) * cores + c for (x, z) in chips for c in range(cores)]
    pairs = [(ring[i], ring[(i + 1) % count]) for i in range(count)]
    place = [0] * count
    for i, d in enumerate(ring):
        place[d] = i
    place = jnp.array(place, jnp.int32)
    my_place = place[dict_index()]
    pieces = [block]
    moving = block
    for _ in range(count - 1):
        moving = lax.ppermute(moving, DICT, pairs)
        pieces.append(moving)
    order = (my_place - place) % count
    ordered = jnp.take(jnp.stack(pieces), order, axis=0)
    return ordered.reshape(count * block.shape[0], block.shape[1])


def fetch_blocks(decoder, block_ids):
    dict_pos = dict_index()
    dict_count = dict_size()
    blocks = []
    for number in range(ABLATION_STEPS):
        dec_rows, owner_dict = owner_rows(decoder, block_ids[number])
        blocks.append(jnp.where(dict_pos == owner_dict, dec_rows, jnp.zeros_like(dec_rows)))
    held = jnp.stack(blocks)
    step = 1
    while step < dict_count:
        pairs = [(i, i ^ step) for i in range(dict_count)]
        held = held + lax.ppermute(held, DICT, pairs)
        step *= 2
    return held


def body(
    residual,
    norm_gain,
    w_query,
    w_key,
    value_weight,
    w_out,
    decoder,
    block_ids,
    latent_ids,
    latent_vals,
    prompt_lens,
):
    row_count = residual.shape[0]
    col_count = residual.shape[1]
    tensor_pos = lax.axis_index("tensor")
    tensor_count = lax.axis_size("tensor")
    full_width = col_count * tensor_count
    head_cols = w_query.shape[1]
    heads_dev = head_cols // HEAD_SIZE
    query_group_size = QUERY_HEADS // KEY_VALUE_HEADS
    kv_index = tensor_pos * heads_dev // query_group_size
    assert 2 * heads_dev <= query_group_size
    is_key_side = tensor_pos % 2 == 0
    key_cols = lax.dynamic_slice_in_dim(w_key, kv_index * HEAD_SIZE, HEAD_SIZE, 1)
    value_cols = lax.dynamic_slice_in_dim(value_weight, kv_index * HEAD_SIZE, HEAD_SIZE, 1)
    kv_cols = jnp.where(is_key_side, key_cols, value_cols)
    packed = jnp.concatenate([w_query, kv_cols], axis=1)
    gathered = lax.all_gather(packed, DICT, axis=0, tiled=True)
    out_rows = ring_gather_dict(w_out.T)
    coef_list = [
        dense_codes(latent_ids, latent_vals, block_ids[number] * BLOCK)
        for number in range(ABLATION_STEPS)
    ]
    col_list = []
    dec_blocks = fetch_blocks(decoder, block_ids)
    for number in range(ABLATION_STEPS):
        dec_slice = dec_blocks[number]
        removed = jnp.dot(coef_list[number], dec_slice, preferred_element_type=jnp.float32)
        col_list.append((residual.astype(jnp.float32) - removed).astype(jnp.bfloat16))
    own_cols = jnp.stack(col_list)
    widened = own_cols.astype(jnp.float32)
    sum_sq = butterfly_sum(jnp.sum(widened * widened, axis=-1, keepdims=True), "tensor", tensor_count)
    mean_sq = sum_sq / full_width
    gain_cols = lax.dynamic_slice_in_dim(norm_gain, tensor_pos * col_count, col_count)
    normed_cols = (widened * lax.rsqrt(mean_sq + EPSILON) * gain_cols).astype(jnp.bfloat16)
    normed_cols, gathered = lax.optimization_barrier((normed_cols, gathered))
    normed = lax.all_gather(normed_cols, "tensor", axis=2, tiled=True)
    normed = normed.reshape(ABLATION_STEPS * row_count, full_width)
    qkv_cols = head_cols + HEAD_SIZE
    qkv = jnp.dot(normed, gathered, preferred_element_type=jnp.float32)
    query_vec = qkv[:, :head_cols]
    kv_vector = qkv[:, head_cols:qkv_cols]
    prompt_count = row_count // PROMPT_ROWS
    cosine_table, sine_table = rope_tables(PROMPT_ROWS, HEAD_SIZE)
    query_vec = apply_rotary(
        query_vec.reshape(ABLATION_STEPS, prompt_count, PROMPT_ROWS, heads_dev, HEAD_SIZE),
        cosine_table[:, None, :],
        sine_table[:, None, :],
    ).astype(jnp.bfloat16)
    kv_vector = kv_vector.reshape(ABLATION_STEPS, prompt_count, PROMPT_ROWS, HEAD_SIZE)
    kv_rotated = apply_rotary(kv_vector, cosine_table, sine_table)
    own_kv = jnp.where(is_key_side, kv_rotated, kv_vector).astype(jnp.bfloat16)
    tensor_pairs = [(i, i ^ 1) for i in range(tensor_count)]
    other_kv = lax.ppermute(own_kv, "tensor", tensor_pairs)
    key_vector = jnp.where(is_key_side, own_kv, other_kv)
    value_vector = jnp.where(is_key_side, other_kv, own_kv)
    positions = jnp.arange(PROMPT_ROWS, dtype=jnp.int32)
    scores = jnp.einsum(
        "spqhd,spkd->sphqk", query_vec, key_vector, preferred_element_type=jnp.float32
    ) / math.sqrt(HEAD_SIZE)
    allowed = (positions[None, None, :] <= positions[None, :, None]) & (
        positions[None, None, :] < prompt_lens[:, None, None]
    )
    scores = jnp.where(allowed[None, :, None, :, :], scores, MASKED)
    weights = jax.nn.softmax(scores, axis=-1).astype(jnp.bfloat16)
    context = jnp.einsum(
        "sphqk,spkd->spqhd", weights, value_vector, preferred_element_type=jnp.float32
    )
    context = context.astype(jnp.bfloat16).reshape(ABLATION_STEPS * row_count, head_cols)
    partial_value = lax.dot_general(
        context,
        out_rows,
        (((1,), (1,)), ((), ())),
        preferred_element_type=jnp.float32,
    ).astype(jnp.bfloat16)
    summed = lax.psum_scatter(
        partial_value.astype(jnp.float32).astype(jnp.bfloat16),
        "tensor",
        scatter_dimension=1,
        tiled=True,
    ).astype(jnp.float32)
    result = own_cols.reshape(ABLATION_STEPS * row_count, col_count).astype(jnp.float32) + summed
    return result.astype(jnp.bfloat16).reshape(ABLATION_STEPS, row_count, col_count)


def solution(mesh):
    dict_count = mesh.shape["dict"]
    core_count = 2 if dict_count % 2 == 0 else 1
    devices = mesh.devices.reshape(dict_count // core_count, core_count, mesh.shape["tensor"])
    fine = jax.sharding.Mesh(devices, ("dict_hi", "core", "tensor"))
    in_specs = (
        P(DICT, "tensor"),
        P(),
        P(DICT, "tensor"),
        P(DICT, None),
        P(DICT, None),
        P("tensor", DICT),
        P(DICT, "tensor"),
        P(),
        P(DICT, None),
        P(DICT, None),
        P(DICT),
    )
    out_specs = P(None, DICT, "tensor")
    return jax.shard_map(body, mesh=fine, in_specs=in_specs, out_specs=out_specs, check_vma=False)
```

```python
import math

import jax
import jax.numpy as jnp
from jax import lax
from jax.sharding import PartitionSpec as P

QUERY_HEADS = 64
KEY_VALUE_HEADS = 8
HEAD_SIZE = 128
BLOCK = 128
PROMPT_ROWS = 256
ABLATION_STEPS = 2


ROPE_BASE = 1000000.0
EPSILON = 1e-06
MASKED = -1e30


def rope_tables(length, head_dim):
    frequency = ROPE_BASE ** (-(jnp.arange(head_dim // 2, dtype=jnp.float32) * 2.0) / head_dim)
    angles = jnp.arange(length, dtype=jnp.float32)[:, None] * frequency[None, :]
    angles = jnp.concatenate([angles, angles], axis=-1)
    return (jnp.cos(angles), jnp.sin(angles))


def apply_rotary(feature_map, cosine_table, sine_table):
    half_width = feature_map.shape[-1] // 2
    first_half = feature_map[..., :half_width]
    second_half = feature_map[..., half_width:]
    turned = jnp.concatenate([-second_half, first_half], axis=-1)
    return feature_map * cosine_table + turned * sine_table


def dense_codes(latent_ids, latent_vals, first_latent):
    offsets = latent_ids - first_latent
    columns = jnp.arange(BLOCK, dtype=jnp.int32)
    matched = offsets[:, :, None] == columns[None, None, :]
    picked = jnp.where(matched, latent_vals[:, :, None], jnp.zeros((), jnp.float32))
    return jnp.sum(picked, axis=1).astype(jnp.bfloat16)


def owner_rows(decoder, block_num):
    lat_count = decoder.shape[0]
    first_latent = block_num * BLOCK
    owner_dict = first_latent // lat_count
    row_offset = first_latent - owner_dict * lat_count
    return (lax.dynamic_slice_in_dim(decoder, row_offset, BLOCK, 0), owner_dict)


DICT = ("dict_hi", "core")


def dict_index():
    return lax.axis_index("dict_hi") * lax.axis_size("core") + lax.axis_index("core")


def dict_size():
    return lax.axis_size("dict_hi") * lax.axis_size("core")


def butterfly_sum(value, axis, count):
    step = 1
    while step < count:
        pairs = [(i, i ^ step) for i in range(count)]
        value = value + lax.ppermute(value, axis, pairs)
        step *= 2
    return value


def fetch_blocks(decoder, block_ids):
    dict_pos = dict_index()
    dict_count = dict_size()
    blocks = []
    for number in range(ABLATION_STEPS):
        dec_rows, owner_dict = owner_rows(decoder, block_ids[number])
        blocks.append(jnp.where(dict_pos == owner_dict, dec_rows, jnp.zeros_like(dec_rows)))
    held = jnp.stack(blocks)
    step = 1
    while step < dict_count:
        pairs = [(i, i ^ step) for i in range(dict_count)]
        held = held + lax.ppermute(held, DICT, pairs)
        step *= 2
    return held


def body(
    residual,
    norm_gain,
    w_query,
    w_key,
    value_weight,
    w_out,
    decoder,
    block_ids,
    latent_ids,
    latent_vals,
    prompt_lens,
):
    row_count = residual.shape[0]
    col_count = residual.shape[1]
    tensor_pos = lax.axis_index("tensor")
    tensor_count = lax.axis_size("tensor")
    full_width = col_count * tensor_count
    head_cols = w_query.shape[1]
    heads_dev = head_cols // HEAD_SIZE
    query_group_size = QUERY_HEADS // KEY_VALUE_HEADS
    kv_index = tensor_pos * heads_dev // query_group_size
    assert 2 * heads_dev <= query_group_size
    is_key_side = tensor_pos % 2 == 0
    key_cols = lax.dynamic_slice_in_dim(w_key, kv_index * HEAD_SIZE, HEAD_SIZE, 1)
    value_cols = lax.dynamic_slice_in_dim(value_weight, kv_index * HEAD_SIZE, HEAD_SIZE, 1)
    kv_cols = jnp.where(is_key_side, key_cols, value_cols)
    packed = jnp.concatenate([w_query, kv_cols], axis=1)
    gathered = lax.all_gather(packed, DICT, axis=0, tiled=True)
    coef_list = [
        dense_codes(latent_ids, latent_vals, block_ids[number] * BLOCK)
        for number in range(ABLATION_STEPS)
    ]
    col_list = []
    dec_blocks = fetch_blocks(decoder, block_ids)
    for number in range(ABLATION_STEPS):
        dec_slice = dec_blocks[number]
        removed = jnp.dot(coef_list[number], dec_slice, preferred_element_type=jnp.float32)
        col_list.append((residual.astype(jnp.float32) - removed).astype(jnp.bfloat16))
    own_cols = jnp.stack(col_list)
    widened = own_cols.astype(jnp.float32)
    sum_sq = butterfly_sum(jnp.sum(widened * widened, axis=-1, keepdims=True), "tensor", tensor_count)
    mean_sq = sum_sq / full_width
    gain_cols = lax.dynamic_slice_in_dim(norm_gain, tensor_pos * col_count, col_count)
    normed_cols = (widened * lax.rsqrt(mean_sq + EPSILON) * gain_cols).astype(jnp.bfloat16)
    normed_cols, gathered = lax.optimization_barrier((normed_cols, gathered))
    normed = lax.all_gather(normed_cols, "tensor", axis=2, tiled=True)
    normed, out_local = lax.optimization_barrier((normed, w_out.T))
    out_rows = lax.all_gather(out_local, DICT, axis=0, tiled=True)
    normed = normed.reshape(ABLATION_STEPS * row_count, full_width)
    qkv_cols = head_cols + HEAD_SIZE
    qkv = jnp.dot(normed, gathered, preferred_element_type=jnp.float32)
    query_vec = qkv[:, :head_cols]
    kv_vector = qkv[:, head_cols:qkv_cols]
    prompt_count = row_count // PROMPT_ROWS
    cosine_table, sine_table = rope_tables(PROMPT_ROWS, HEAD_SIZE)
    query_vec = apply_rotary(
        query_vec.reshape(ABLATION_STEPS, prompt_count, PROMPT_ROWS, heads_dev, HEAD_SIZE),
        cosine_table[:, None, :],
        sine_table[:, None, :],
    ).astype(jnp.bfloat16)
    kv_vector = kv_vector.reshape(ABLATION_STEPS, prompt_count, PROMPT_ROWS, HEAD_SIZE)
    kv_rotated = apply_rotary(kv_vector, cosine_table, sine_table)
    own_kv = jnp.where(is_key_side, kv_rotated, kv_vector).astype(jnp.bfloat16)
    tensor_pairs = [(i, i ^ 1) for i in range(tensor_count)]
    other_kv = lax.ppermute(own_kv, "tensor", tensor_pairs)
    key_vector = jnp.where(is_key_side, own_kv, other_kv)
    value_vector = jnp.where(is_key_side, other_kv, own_kv)
    positions = jnp.arange(PROMPT_ROWS, dtype=jnp.int32)
    scores = jnp.einsum(
        "spqhd,spkd->sphqk", query_vec, key_vector, preferred_element_type=jnp.float32
    ) / math.sqrt(HEAD_SIZE)
    allowed = (positions[None, None, :] <= positions[None, :, None]) & (
        positions[None, None, :] < prompt_lens[:, None, None]
    )
    scores = jnp.where(allowed[None, :, None, :, :], scores, MASKED)
    weights = jax.nn.softmax(scores, axis=-1).astype(jnp.bfloat16)
    context = jnp.einsum(
        "sphqk,spkd->spqhd", weights, value_vector, preferred_element_type=jnp.float32
    )
    context = context.astype(jnp.bfloat16).reshape(ABLATION_STEPS * row_count, head_cols)
    partial_value = lax.dot_general(
        context,
        out_rows,
        (((1,), (1,)), ((), ())),
        preferred_element_type=jnp.float32,
    ).astype(jnp.bfloat16)
    summed = lax.psum_scatter(
        partial_value.astype(jnp.float32).astype(jnp.bfloat16),
        "tensor",
        scatter_dimension=1,
        tiled=True,
    ).astype(jnp.float32)
    result = own_cols.reshape(ABLATION_STEPS * row_count, col_count).astype(jnp.float32) + summed
    return result.astype(jnp.bfloat16).reshape(ABLATION_STEPS, row_count, col_count)


def solution(mesh):
    dict_count = mesh.shape["dict"]
    core_count = 2 if dict_count % 2 == 0 else 1
    devices = mesh.devices.reshape(dict_count // core_count, core_count, mesh.shape["tensor"])
    fine = jax.sharding.Mesh(devices, ("dict_hi", "core", "tensor"))
    in_specs = (
        P(DICT, "tensor"),
        P(),
        P(DICT, "tensor"),
        P(DICT, None),
        P(DICT, None),
        P("tensor", DICT),
        P(DICT, "tensor"),
        P(),
        P(DICT, None),
        P(DICT, None),
        P(DICT),
    )
    out_specs = P(None, DICT, "tensor")
    return jax.shard_map(body, mesh=fine, in_specs=in_specs, out_specs=out_specs, check_vma=False)
```

```python
import math

import jax
import jax.numpy as jnp
from jax import lax
from jax.sharding import PartitionSpec as P

QUERY_HEADS = 64
KEY_VALUE_HEADS = 8
HEAD_SIZE = 128
BLOCK = 128
PROMPT_ROWS = 256
ABLATION_STEPS = 2


ROPE_BASE = 1000000.0
EPSILON = 1e-06
MASKED = -1e30


def rope_tables(length, head_dim):
    frequency = ROPE_BASE ** (-(jnp.arange(head_dim // 2, dtype=jnp.float32) * 2.0) / head_dim)
    angles = jnp.arange(length, dtype=jnp.float32)[:, None] * frequency[None, :]
    angles = jnp.concatenate([angles, angles], axis=-1)
    return (jnp.cos(angles), jnp.sin(angles))


def apply_rotary(feature_map, cosine_table, sine_table):
    half_width = feature_map.shape[-1] // 2
    first_half = feature_map[..., :half_width]
    second_half = feature_map[..., half_width:]
    turned = jnp.concatenate([-second_half, first_half], axis=-1)
    return feature_map * cosine_table + turned * sine_table


def dense_codes(latent_ids, latent_vals, first_latent):
    offsets = latent_ids - first_latent
    columns = jnp.arange(BLOCK, dtype=jnp.int32)
    matched = offsets[:, :, None] == columns[None, None, :]
    picked = jnp.where(matched, latent_vals[:, :, None], jnp.zeros((), jnp.float32))
    return jnp.sum(picked, axis=1).astype(jnp.bfloat16)


def owner_rows(decoder, block_num):
    lat_count = decoder.shape[0]
    first_latent = block_num * BLOCK
    owner_dict = first_latent // lat_count
    row_offset = first_latent - owner_dict * lat_count
    return (lax.dynamic_slice_in_dim(decoder, row_offset, BLOCK, 0), owner_dict)


DICT = ("dict_x", "dict_z", "core")
DICT_RING = ("dict_z", "dict_x", "core")


def dict_index():
    return (lax.axis_index("dict_x") * lax.axis_size("dict_z") + lax.axis_index("dict_z")) * lax.axis_size(
        "core"
    ) + lax.axis_index("core")


def dict_size():
    return lax.axis_size("dict_x") * lax.axis_size("dict_z") * lax.axis_size("core")


def butterfly_sum(value, axis, count):
    step = 1
    while step < count:
        pairs = [(i, i ^ step) for i in range(count)]
        value = value + lax.ppermute(value, axis, pairs)
        step *= 2
    return value


def fetch_blocks(decoder, block_ids):
    dict_pos = dict_index()
    dict_count = dict_size()
    blocks = []
    for number in range(ABLATION_STEPS):
        dec_rows, owner_dict = owner_rows(decoder, block_ids[number])
        blocks.append(jnp.where(dict_pos == owner_dict, dec_rows, jnp.zeros_like(dec_rows)))
    held = jnp.stack(blocks)
    step = 1
    while step < dict_count:
        pairs = [(i, i ^ step) for i in range(dict_count)]
        held = held + lax.ppermute(held, DICT, pairs)
        step *= 2
    return held


def body(
    residual,
    norm_gain,
    w_query,
    w_key,
    value_weight,
    w_out,
    decoder,
    block_ids,
    latent_ids,
    latent_vals,
    prompt_lens,
):
    row_count = residual.shape[0]
    col_count = residual.shape[1]
    tensor_pos = lax.axis_index("tensor")
    tensor_count = lax.axis_size("tensor")
    full_width = col_count * tensor_count
    head_cols = w_query.shape[1]
    heads_dev = head_cols // HEAD_SIZE
    query_group_size = QUERY_HEADS // KEY_VALUE_HEADS
    kv_index = tensor_pos * heads_dev // query_group_size
    assert 2 * heads_dev <= query_group_size
    is_key_side = tensor_pos % 2 == 0
    key_cols = lax.dynamic_slice_in_dim(w_key, kv_index * HEAD_SIZE, HEAD_SIZE, 1)
    value_cols = lax.dynamic_slice_in_dim(value_weight, kv_index * HEAD_SIZE, HEAD_SIZE, 1)
    kv_cols = jnp.where(is_key_side, key_cols, value_cols)
    packed = jnp.concatenate([w_query, kv_cols, w_out.T], axis=1)
    ring_gathered = lax.all_gather(packed, DICT_RING, axis=0, tiled=True)
    coef_list = [
        dense_codes(latent_ids, latent_vals, block_ids[number] * BLOCK)
        for number in range(ABLATION_STEPS)
    ]
    col_list = []
    dec_blocks = fetch_blocks(decoder, block_ids)
    for number in range(ABLATION_STEPS):
        dec_slice = dec_blocks[number]
        removed = jnp.dot(coef_list[number], dec_slice, preferred_element_type=jnp.float32)
        col_list.append((residual.astype(jnp.float32) - removed).astype(jnp.bfloat16))
    own_cols = jnp.stack(col_list)
    widened = own_cols.astype(jnp.float32)
    sum_sq = butterfly_sum(jnp.sum(widened * widened, axis=-1, keepdims=True), "tensor", tensor_count)
    mean_sq = sum_sq / full_width
    gain_cols = lax.dynamic_slice_in_dim(norm_gain, tensor_pos * col_count, col_count)
    normed_cols = (widened * lax.rsqrt(mean_sq + EPSILON) * gain_cols).astype(jnp.bfloat16)
    normed_cols, ring_gathered = lax.optimization_barrier((normed_cols, ring_gathered))
    x_count = lax.axis_size("dict_x")
    z_count = lax.axis_size("dict_z")
    core_count = lax.axis_size("core")
    gathered = ring_gathered.reshape((z_count, x_count, core_count) + packed.shape)
    gathered = jnp.transpose(gathered, (1, 0, 2, 3, 4)).reshape(-1, packed.shape[1])
    normed = lax.all_gather(normed_cols, "tensor", axis=2, tiled=True)
    normed = normed.reshape(ABLATION_STEPS * row_count, full_width)
    qkv_cols = head_cols + HEAD_SIZE
    qkv = jnp.dot(normed, gathered[:, :qkv_cols], preferred_element_type=jnp.float32)
    query_vec = qkv[:, :head_cols]
    kv_vector = qkv[:, head_cols:qkv_cols]
    prompt_count = row_count // PROMPT_ROWS
    cosine_table, sine_table = rope_tables(PROMPT_ROWS, HEAD_SIZE)
    query_vec = apply_rotary(
        query_vec.reshape(ABLATION_STEPS, prompt_count, PROMPT_ROWS, heads_dev, HEAD_SIZE),
        cosine_table[:, None, :],
        sine_table[:, None, :],
    ).astype(jnp.bfloat16)
    kv_vector = kv_vector.reshape(ABLATION_STEPS, prompt_count, PROMPT_ROWS, HEAD_SIZE)
    kv_rotated = apply_rotary(kv_vector, cosine_table, sine_table)
    own_kv = jnp.where(is_key_side, kv_rotated, kv_vector).astype(jnp.bfloat16)
    tensor_pairs = [(i, i ^ 1) for i in range(tensor_count)]
    other_kv = lax.ppermute(own_kv, "tensor", tensor_pairs)
    key_vector = jnp.where(is_key_side, own_kv, other_kv)
    value_vector = jnp.where(is_key_side, other_kv, own_kv)
    positions = jnp.arange(PROMPT_ROWS, dtype=jnp.int32)
    scores = jnp.einsum(
        "spqhd,spkd->sphqk", query_vec, key_vector, preferred_element_type=jnp.float32
    ) / math.sqrt(HEAD_SIZE)
    allowed = (positions[None, None, :] <= positions[None, :, None]) & (
        positions[None, None, :] < prompt_lens[:, None, None]
    )
    scores = jnp.where(allowed[None, :, None, :, :], scores, MASKED)
    weights = jax.nn.softmax(scores, axis=-1).astype(jnp.bfloat16)
    context = jnp.einsum(
        "sphqk,spkd->spqhd", weights, value_vector, preferred_element_type=jnp.float32
    )
    context = context.astype(jnp.bfloat16).reshape(ABLATION_STEPS * row_count, head_cols)
    partial_value = lax.dot_general(
        context,
        gathered[:, qkv_cols:],
        (((1,), (1,)), ((), ())),
        preferred_element_type=jnp.float32,
    ).astype(jnp.bfloat16)
    summed = lax.psum_scatter(
        partial_value.astype(jnp.float32).astype(jnp.bfloat16),
        "tensor",
        scatter_dimension=1,
        tiled=True,
    ).astype(jnp.float32)
    result = own_cols.reshape(ABLATION_STEPS * row_count, col_count).astype(jnp.float32) + summed
    return result.astype(jnp.bfloat16).reshape(ABLATION_STEPS, row_count, col_count)


def solution(mesh):
    dict_count = mesh.shape["dict"]
    core_count = 2 if dict_count % 2 == 0 else 1
    z_count = 2 if dict_count % (2 * core_count) == 0 else 1
    x_count = dict_count // (core_count * z_count)
    devices = mesh.devices.reshape(x_count, z_count, core_count, mesh.shape["tensor"])
    fine = jax.sharding.Mesh(devices, ("dict_x", "dict_z", "core", "tensor"))
    in_specs = (
        P(DICT, "tensor"),
        P(),
        P(DICT, "tensor"),
        P(DICT, None),
        P(DICT, None),
        P("tensor", DICT),
        P(DICT, "tensor"),
        P(),
        P(DICT, None),
        P(DICT, None),
        P(DICT),
    )
    out_specs = P(None, DICT, "tensor")
    return jax.shard_map(body, mesh=fine, in_specs=in_specs, out_specs=out_specs, check_vma=False)
```

```python
import math

import jax
import jax.numpy as jnp
from jax import lax
from jax.sharding import PartitionSpec as P

QUERY_HEADS = 64
KEY_VALUE_HEADS = 8
HEAD_SIZE = 128
BLOCK = 128
PROMPT_ROWS = 256
ABLATION_STEPS = 2


ROPE_BASE = 1000000.0
EPSILON = 1e-06
MASKED = -1e30


def rope_tables(length, head_dim):
    frequency = ROPE_BASE ** (-(jnp.arange(head_dim // 2, dtype=jnp.float32) * 2.0) / head_dim)
    angles = jnp.arange(length, dtype=jnp.float32)[:, None] * frequency[None, :]
    angles = jnp.concatenate([angles, angles], axis=-1)
    return (jnp.cos(angles), jnp.sin(angles))


def apply_rotary(feature_map, cosine_table, sine_table):
    half_width = feature_map.shape[-1] // 2
    first_half = feature_map[..., :half_width]
    second_half = feature_map[..., half_width:]
    turned = jnp.concatenate([-second_half, first_half], axis=-1)
    return feature_map * cosine_table + turned * sine_table


def dense_codes(latent_ids, latent_vals, first_latent):
    offsets = latent_ids - first_latent
    columns = jnp.arange(BLOCK, dtype=jnp.int32)
    matched = offsets[:, :, None] == columns[None, None, :]
    picked = jnp.where(matched, latent_vals[:, :, None], jnp.zeros((), jnp.float32))
    return jnp.sum(picked, axis=1).astype(jnp.bfloat16)


def owner_rows(decoder, block_num):
    lat_count = decoder.shape[0]
    first_latent = block_num * BLOCK
    owner_dict = first_latent // lat_count
    row_offset = first_latent - owner_dict * lat_count
    return (lax.dynamic_slice_in_dim(decoder, row_offset, BLOCK, 0), owner_dict)


DICT = ("dict_x", "dict_z", "core")
DICT_RING = ("dict_z", "core", "dict_x")


def dict_index():
    return (lax.axis_index("dict_x") * lax.axis_size("dict_z") + lax.axis_index("dict_z")) * lax.axis_size(
        "core"
    ) + lax.axis_index("core")


def dict_size():
    return lax.axis_size("dict_x") * lax.axis_size("dict_z") * lax.axis_size("core")


def butterfly_sum(value, axis, count):
    step = 1
    while step < count:
        pairs = [(i, i ^ step) for i in range(count)]
        value = value + lax.ppermute(value, axis, pairs)
        step *= 2
    return value


def fetch_blocks(decoder, block_ids):
    dict_pos = dict_index()
    dict_count = dict_size()
    blocks = []
    for number in range(ABLATION_STEPS):
        dec_rows, owner_dict = owner_rows(decoder, block_ids[number])
        blocks.append(jnp.where(dict_pos == owner_dict, dec_rows, jnp.zeros_like(dec_rows)))
    held = jnp.stack(blocks)
    step = 1
    while step < dict_count:
        pairs = [(i, i ^ step) for i in range(dict_count)]
        held = held + lax.ppermute(held, DICT, pairs)
        step *= 2
    return held


def body(
    residual,
    norm_gain,
    w_query,
    w_key,
    value_weight,
    w_out,
    decoder,
    block_ids,
    latent_ids,
    latent_vals,
    prompt_lens,
):
    row_count = residual.shape[0]
    col_count = residual.shape[1]
    tensor_pos = lax.axis_index("tensor")
    tensor_count = lax.axis_size("tensor")
    full_width = col_count * tensor_count
    head_cols = w_query.shape[1]
    heads_dev = head_cols // HEAD_SIZE
    query_group_size = QUERY_HEADS // KEY_VALUE_HEADS
    kv_index = tensor_pos * heads_dev // query_group_size
    assert 2 * heads_dev <= query_group_size
    is_key_side = tensor_pos % 2 == 0
    key_cols = lax.dynamic_slice_in_dim(w_key, kv_index * HEAD_SIZE, HEAD_SIZE, 1)
    value_cols = lax.dynamic_slice_in_dim(value_weight, kv_index * HEAD_SIZE, HEAD_SIZE, 1)
    kv_cols = jnp.where(is_key_side, key_cols, value_cols)
    packed = jnp.concatenate([w_query, kv_cols, w_out.T], axis=1)
    ring_gathered = lax.all_gather(packed, DICT_RING, axis=0, tiled=True)
    coef_list = [
        dense_codes(latent_ids, latent_vals, block_ids[number] * BLOCK)
        for number in range(ABLATION_STEPS)
    ]
    col_list = []
    dec_blocks = fetch_blocks(decoder, block_ids)
    for number in range(ABLATION_STEPS):
        dec_slice = dec_blocks[number]
        removed = jnp.dot(coef_list[number], dec_slice, preferred_element_type=jnp.float32)
        col_list.append((residual.astype(jnp.float32) - removed).astype(jnp.bfloat16))
    own_cols = jnp.stack(col_list)
    widened = own_cols.astype(jnp.float32)
    sum_sq = butterfly_sum(jnp.sum(widened * widened, axis=-1, keepdims=True), "tensor", tensor_count)
    mean_sq = sum_sq / full_width
    gain_cols = lax.dynamic_slice_in_dim(norm_gain, tensor_pos * col_count, col_count)
    normed_cols = (widened * lax.rsqrt(mean_sq + EPSILON) * gain_cols).astype(jnp.bfloat16)
    normed_cols, ring_gathered = lax.optimization_barrier((normed_cols, ring_gathered))
    x_count = lax.axis_size("dict_x")
    z_count = lax.axis_size("dict_z")
    core_count = lax.axis_size("core")
    gathered = ring_gathered.reshape((z_count, core_count, x_count) + packed.shape)
    gathered = jnp.transpose(gathered, (2, 0, 1, 3, 4)).reshape(-1, packed.shape[1])
    normed = lax.all_gather(normed_cols, "tensor", axis=2, tiled=True)
    normed = normed.reshape(ABLATION_STEPS * row_count, full_width)
    qkv_cols = head_cols + HEAD_SIZE
    qkv = jnp.dot(normed, gathered[:, :qkv_cols], preferred_element_type=jnp.float32)
    query_vec = qkv[:, :head_cols]
    kv_vector = qkv[:, head_cols:qkv_cols]
    prompt_count = row_count // PROMPT_ROWS
    cosine_table, sine_table = rope_tables(PROMPT_ROWS, HEAD_SIZE)
    query_vec = apply_rotary(
        query_vec.reshape(ABLATION_STEPS, prompt_count, PROMPT_ROWS, heads_dev, HEAD_SIZE),
        cosine_table[:, None, :],
        sine_table[:, None, :],
    ).astype(jnp.bfloat16)
    kv_vector = kv_vector.reshape(ABLATION_STEPS, prompt_count, PROMPT_ROWS, HEAD_SIZE)
    kv_rotated = apply_rotary(kv_vector, cosine_table, sine_table)
    own_kv = jnp.where(is_key_side, kv_rotated, kv_vector).astype(jnp.bfloat16)
    tensor_pairs = [(i, i ^ 1) for i in range(tensor_count)]
    other_kv = lax.ppermute(own_kv, "tensor", tensor_pairs)
    key_vector = jnp.where(is_key_side, own_kv, other_kv)
    value_vector = jnp.where(is_key_side, other_kv, own_kv)
    positions = jnp.arange(PROMPT_ROWS, dtype=jnp.int32)
    scores = jnp.einsum(
        "spqhd,spkd->sphqk", query_vec, key_vector, preferred_element_type=jnp.float32
    ) / math.sqrt(HEAD_SIZE)
    allowed = (positions[None, None, :] <= positions[None, :, None]) & (
        positions[None, None, :] < prompt_lens[:, None, None]
    )
    scores = jnp.where(allowed[None, :, None, :, :], scores, MASKED)
    weights = jax.nn.softmax(scores, axis=-1).astype(jnp.bfloat16)
    context = jnp.einsum(
        "sphqk,spkd->spqhd", weights, value_vector, preferred_element_type=jnp.float32
    )
    context = context.astype(jnp.bfloat16).reshape(ABLATION_STEPS * row_count, head_cols)
    partial_value = lax.dot_general(
        context,
        gathered[:, qkv_cols:],
        (((1,), (1,)), ((), ())),
        preferred_element_type=jnp.float32,
    ).astype(jnp.bfloat16)
    summed = lax.psum_scatter(
        partial_value.astype(jnp.float32).astype(jnp.bfloat16),
        "tensor",
        scatter_dimension=1,
        tiled=True,
    ).astype(jnp.float32)
    result = own_cols.reshape(ABLATION_STEPS * row_count, col_count).astype(jnp.float32) + summed
    return result.astype(jnp.bfloat16).reshape(ABLATION_STEPS, row_count, col_count)


def solution(mesh):
    dict_count = mesh.shape["dict"]
    core_count = 2 if dict_count % 2 == 0 else 1
    z_count = 2 if dict_count % (2 * core_count) == 0 else 1
    x_count = dict_count // (core_count * z_count)
    devices = mesh.devices.reshape(x_count, z_count, core_count, mesh.shape["tensor"])
    fine = jax.sharding.Mesh(devices, ("dict_x", "dict_z", "core", "tensor"))
    in_specs = (
        P(DICT, "tensor"),
        P(),
        P(DICT, "tensor"),
        P(DICT, None),
        P(DICT, None),
        P("tensor", DICT),
        P(DICT, "tensor"),
        P(),
        P(DICT, None),
        P(DICT, None),
        P(DICT),
    )
    out_specs = P(None, DICT, "tensor")
    return jax.shard_map(body, mesh=fine, in_specs=in_specs, out_specs=out_specs, check_vma=False)
```
